1024 devices in a mesh: space: 64 (over y, z_lo), chan: 16 (over z_hi, x, core).
Axes of the slice: x: 4, y: 4, z: 32 (z_hi: 2, z_lo: 16; z = z_hi * 16 + z_lo), core: 2. Of those that a mesh axis runs over, the one named last changes fastest.
Arguments:
- latent: bfloat16 [2, 64, 32, 1024], P(None, 'space', None, 'chan'), may hold values from -6 to 6
- conv_one: bfloat16 [27, 1024, 1024], P(None, None, 'chan'), may hold values from -0.0390625 to 0.0390625
- bias_one: float32 [1024], P('chan'), may hold values from -3 to 3
- conv_two: bfloat16 [27, 1024, 1024], P(None, 'chan'), may hold values from -0.0546875 to 0.0546875
- bias_two: float32 [1024], P('chan'), may hold values from -3 to 3
Outputs:
- block_out: bfloat16 [2, 64, 32, 1024], P(None, 'space', None, 'chan')
The draws below stay inside these ranges and needn't reach their ends.
All inputs are finite; a program needn't handle non-finite values.
Results may differ from the reference program's by a relative error of at most 0.0034.
Values may be sent and summed in bfloat16 or wider, within the bound.
No kernel may reach another device: no remote copies, remote signals or barrier semaphores. Data moves between devices by JAX's collectives and lax.ppermute only.
A program may use at most 32 MiB of HBM per device.

```python
import jax
import jax.numpy as jnp

CH = 1024
FRAMES = 2
WIDTH = 32
HEIGHT = 64


def with_spikes(values, rng, source, target, parts, factor):
    owner, partner = [(jnp.arange(values.shape[dim]) // (values.shape[dim] // parts)).reshape([-1 if axis == dim else 1 for axis in range(values.ndim)]) for dim in (source, target)]
    chosen = jax.random.permutation(rng, parts)[partner]
    strong = (owner == chosen) | (owner == (partner + parts // 2) % parts)
    return jnp.where(strong, factor * values, values)


def block_scale(stream_key, dims, pieces, smallest, top_value):
    factor_of = 1.0
    for dim, shards_of in pieces:
        draws = jax.random.uniform(jax.random.fold_in(jax.random.fold_in(stream_key, 6), dim), (shards_of,), jnp.float32, smallest / len(pieces), top_value / len(pieces))
        factor_of = factor_of * jnp.repeat(jnp.exp(draws), dims[dim] // shards_of).reshape((-1,) + (1,) * (len(dims) - 1 - dim))
    return factor_of


def gaussian(own_key, dims, scale, reach, pieces=(), dtype=jnp.bfloat16):
    result = scale * jax.random.normal(own_key, dims, jnp.float32)
    if pieces:
        result = result * block_scale(own_key, dims, pieces, -0.22, 0.18)
    return jnp.clip(result, -reach, reach).astype(dtype)


def noise_with(key, shape, spread, bound, split, heavy, kind=jnp.bfloat16):
    entries = spread * jax.random.normal(key, shape, jnp.float32)
    if split:
        entries = entries * block_scale(key, shape, split, -0.22, 0.18)
    return jnp.clip(with_spikes(entries, jax.random.fold_in(key, 3), *heavy), -bound, bound).astype(kind)


def setup_inputs(seed: int = 0) -> dict:
    arg_keys = jax.random.split(jax.random.key(seed), 6)
    return {
        "latent": gaussian(arg_keys[0], (FRAMES, HEIGHT, WIDTH, CH), 1.0, 6.0, ((1, 64), (3, 16))),
        "conv_one": gaussian(arg_keys[1], (27, CH, CH), (27 * CH) ** -0.5, 0.0390625, ((2, 16),)),
        "bias_one": gaussian(arg_keys[2], (CH,), 0.5, 3.0, ((0, 16),), jnp.float32),
        "conv_two": noise_with(arg_keys[3], (27, CH, CH), (27 * CH) ** -0.5, 0.0546875, ((1, 16),), (1, 2, 16, 2.0)),
        "bias_two": gaussian(arg_keys[4], (CH,), 0.5, 3.0, ((0, 16),), jnp.float32),
    }


def conv_full(values, kernel):
    frame_count, row_count, col_count, in_chan = values.shape
    padded = jnp.pad(values, ((1, 1), (1, 1), (1, 1), (0, 0)))
    accum = jnp.zeros((frame_count * row_count * col_count, kernel.shape[2]), jnp.float32)
    for depth_off in range(3):
        for row_off in range(3):
            for col_off in range(3):
                window = padded[depth_off:depth_off + frame_count, row_off:row_off + row_count, col_off:col_off + col_count]
                flat = window.reshape(frame_count * row_count * col_count, in_chan)
                accum = accum + jnp.dot(flat, kernel[depth_off * 9 + row_off * 3 + col_off], preferred_element_type=jnp.float32)
    return accum.reshape(frame_count, row_count, col_count, kernel.shape[2])


def reference(latent, conv_one, bias_one, conv_two, bias_two):
    hidden = jax.nn.relu(conv_full(latent, conv_one) + bias_one).astype(jnp.bfloat16)
    summed = latent.astype(jnp.float32) + conv_full(hidden, conv_two) + bias_two
    return summed.astype(jnp.bfloat16)
```

```python
import jax
import jax.numpy as jnp
from jax import lax
from jax.sharding import Mesh
from jax.sharding import PartitionSpec as P

CHAN = ("zh", "inner")
HALVES = 2


def halo_rows(cells, dim):
    count = lax.axis_size("space")
    ends = count - 1
    head = lax.slice_in_dim(cells, 0, 1, axis=dim)
    tail = lax.slice_in_dim(cells, cells.shape[dim] - 1, cells.shape[dim], axis=dim)
    return jnp.concatenate(
        [
            lax.ppermute(tail, "space", [(i, (i + 1) % count) for i in range(ends)]),
            cells,
            lax.ppermute(head, "space", [((i + 1) % count, i) for i in range(ends)]),
        ],
        axis=dim,
    )


def swap_halves(v):
    return lax.ppermute(v, "zh", [(0, 1), (1, 0)])


def pad_sides(values):
    return jnp.pad(values, ((1, 1), (0, 0), (1, 1), (0, 0)))


def tap_windows(padded, frame_count, row_count, col_count):
    windows = []
    for depth_off in range(3):
        for row_off in range(3):
            for col_off in range(3):
                window = padded[
                    depth_off : depth_off + frame_count,
                    row_off : row_off + row_count,
                    col_off : col_off + col_count,
                ]
                windows.append(window.reshape(frame_count * row_count * col_count, padded.shape[3]))
    return windows


def tap_sum(padded, kernel, frame_count, row_count, col_count):
    accum = None
    for tap_index, flat in enumerate(tap_windows(padded, frame_count, row_count, col_count)):
        term = jnp.dot(flat, kernel[tap_index], preferred_element_type=jnp.float32)
        accum = term if accum is None else accum + term
    return accum


def gather_channels(latent):
    other = swap_halves(latent)
    half = lax.axis_index("zh")
    pair = jnp.where(half == 0, jnp.stack([latent, other]), jnp.stack([other, latent]))
    inner = lax.all_gather(pair, "inner", axis=0, tiled=False)
    frame_count, row_count, col_count, own_chan = latent.shape
    total = inner.shape[0] * HALVES * own_chan
    return jnp.transpose(inner, (2, 3, 4, 1, 0, 5)).reshape(frame_count, row_count, col_count, total)


def reduce_channels(partial, own_chan):
    inner_count = lax.axis_size("inner")
    cells = partial.shape[1]
    cur = partial.reshape(HALVES, inner_count, own_chan, cells).transpose(1, 0, 2, 3)
    idx = lax.axis_index("inner")
    step = inner_count // 2
    while step >= 1:
        size = cur.shape[0] // 2
        low, high = cur[:size], cur[size:]
        upper = (idx // step) % 2 == 1
        keep = jnp.where(upper, high, low)
        send = jnp.where(upper, low, high)
        cur = keep + lax.ppermute(send, "inner", [(i, i ^ step) for i in range(inner_count)])
        step //= 2
    sums = cur[0]
    half = lax.axis_index("zh")
    mine = jnp.where(half == 0, sums[0], sums[1])
    theirs = jnp.where(half == 0, sums[1], sums[0])
    return mine + swap_halves(theirs)


def local(latent, conv_one, bias_one, conv_two, bias_two):
    frame_count, row_count, col_count, own_chan = latent.shape
    gathered = gather_channels(latent)
    extended = halo_rows(gathered, 1)
    first = tap_sum(pad_sides(extended), conv_one, frame_count, row_count, col_count)
    hidden = jax.nn.relu(first + bias_one).astype(jnp.bfloat16)
    hidden = hidden.reshape(frame_count, row_count, col_count, own_chan)
    hidden_ext = halo_rows(hidden, 1)
    columns = jnp.concatenate(
        tap_windows(pad_sides(hidden_ext), frame_count, row_count, col_count), axis=1
    )
    flat_two = conv_two.reshape(27 * own_chan, conv_two.shape[2])
    partial = lax.dot_general(
        flat_two, columns, (((0,), (1,)), ((), ())), preferred_element_type=jnp.float32
    )
    mine = reduce_channels(partial, own_chan)
    second = mine.T.reshape(frame_count, row_count, col_count, own_chan)
    summed = latent.astype(jnp.float32) + second + bias_two
    return summed.astype(jnp.bfloat16)


def solution(mesh):
    space, chan = mesh.shape["space"], mesh.shape["chan"]
    split = Mesh(mesh.devices.reshape(space, HALVES, chan // HALVES), ("space",) + CHAN)
    in_specs = (
        P(None, "space", None, CHAN),
        P(None, None, CHAN),
        P(CHAN),
        P(None, CHAN, None),
        P(CHAN),
    )
    out_specs = P(None, "space", None, CHAN)
    return jax.shard_map(local, mesh=split, in_specs=in_specs, out_specs=out_specs, check_vma=False)
```

```python
import jax
import jax.numpy as jnp
from jax import lax
from jax.sharding import Mesh
from jax.sharding import PartitionSpec as P

CHAN = ("zh", "inner")
HALVES = 2
RUN = 16


def row_from(cells, shift):
    rows = lax.axis_size("space")
    pairs = []
    for target in range(rows):
        source = target + shift
        if 0 <= source < rows:
            cross = source // RUN != target // RUN
            for half in range(HALVES):
                other = (HALVES - 1 - half) if cross else half
                pairs.append((source * HALVES + other, target * HALVES + half))
    return lax.ppermute(cells, ("space", "zh"), pairs)


def halo_rows(cells, width):
    parts = [row_from(cells, -d) for d in range(width, 0, -1)]
    parts += [cells] + [row_from(cells, d) for d in range(1, width + 1)]
    return jnp.concatenate(parts, axis=1)


def swap_halves(v):
    return lax.ppermute(v, "zh", [(0, 1), (1, 0)])


def pad_sides(values):
    return jnp.pad(values, ((1, 1), (0, 0), (1, 1), (0, 0)))


def tap_windows(padded, frame_count, row_count, col_count):
    windows = []
    for depth_off in range(3):
        for row_off in range(3):
            for col_off in range(3):
                window = padded[
                    depth_off : depth_off + frame_count,
                    row_off : row_off + row_count,
                    col_off : col_off + col_count,
                ]
                windows.append(window.reshape(frame_count * row_count * col_count, padded.shape[3]))
    return windows


def tap_sum(padded, kernel, frame_count, row_count, col_count):
    accum = None
    for tap_index, flat in enumerate(tap_windows(padded, frame_count, row_count, col_count)):
        term = jnp.dot(flat, kernel[tap_index], preferred_element_type=jnp.float32)
        accum = term if accum is None else accum + term
    return accum


def gather_channels(latent):
    other = swap_halves(latent)
    half = lax.axis_index("zh")
    pair = jnp.where(half == 0, jnp.stack([latent, other]), jnp.stack([other, latent]))
    inner_count = lax.axis_size("inner")
    copies = jnp.broadcast_to(pair[None], (inner_count,) + pair.shape)
    inner = lax.all_to_all(copies, "inner", 0, 0, tiled=True)
    frame_count, row_count, col_count, own_chan = latent.shape
    total = inner.shape[0] * HALVES * own_chan
    return jnp.transpose(inner, (2, 3, 4, 1, 0, 5)).reshape(frame_count, row_count, col_count, total)


def reduce_channels(partial, own_chan):
    inner_count = lax.axis_size("inner")
    cells = partial.shape[1]
    blocks = partial.reshape(HALVES, inner_count, own_chan, cells).transpose(1, 0, 2, 3)
    sums = lax.all_to_all(blocks, "inner", 0, 0, tiled=True).sum(0)
    half = lax.axis_index("zh")
    mine = jnp.where(half == 0, sums[0], sums[1])
    theirs = jnp.where(half == 0, sums[1], sums[0])
    return mine + swap_halves(theirs)


def local(latent, conv_one, bias_one, conv_two, bias_two):
    frame_count, row_count, col_count, own_chan = latent.shape
    gathered = gather_channels(latent)
    extended = halo_rows(gathered, 2)
    first = tap_sum(pad_sides(extended), conv_one, frame_count, row_count + 2, col_count)
    hidden = jax.nn.relu(first + bias_one).astype(jnp.bfloat16)
    hidden = hidden.reshape(frame_count, row_count + 2, col_count, own_chan)
    row = lax.axis_index("space") * row_count + jnp.arange(-1, row_count + 1)
    inside = (row >= 0) & (row < lax.axis_size("space") * row_count)
    hidden_ext = jnp.where(inside[None, :, None, None], hidden, jnp.zeros_like(hidden))
    columns = jnp.concatenate(
        tap_windows(pad_sides(hidden_ext), frame_count, row_count, col_count), axis=1
    )
    flat_two = conv_two.reshape(27 * own_chan, conv_two.shape[2])
    partial = lax.dot_general(
        flat_two, columns, (((0,), (1,)), ((), ())), preferred_element_type=jnp.float32
    )
    mine = reduce_channels(partial, own_chan)
    second = mine.T.reshape(frame_count, row_count, col_count, own_chan)
    summed = latent.astype(jnp.float32) + second + bias_two
    return summed.astype(jnp.bfloat16)


def solution(mesh):
    space, chan = mesh.shape["space"], mesh.shape["chan"]
    split = Mesh(mesh.devices.reshape(space, HALVES, chan // HALVES), ("space",) + CHAN)
    in_specs = (
        P(None, "space", None, CHAN),
        P(None, None, CHAN),
        P(CHAN),
        P(None, CHAN, None),
        P(CHAN),
    )
    out_specs = P(None, "space", None, CHAN)
    return jax.shard_map(local, mesh=split, in_specs=in_specs, out_specs=out_specs, check_vma=False)
```

```python
import jax
import jax.numpy as jnp
from jax import lax
from jax.sharding import Mesh
from jax.sharding import PartitionSpec as P

CHAN = ("zh", "inner")
HALVES = 2
RUN = 16


def row_from(cells, shift):
    rows = lax.axis_size("space")
    pairs = []
    for target in range(rows):
        source = target + shift
        if 0 <= source < rows:
            cross = source // RUN != target // RUN
            for half in range(HALVES):
                other = (HALVES - 1 - half) if cross else half
                pairs.append((source * HALVES + other, target * HALVES + half))
    return lax.ppermute(cells, ("space", "zh"), pairs)


def halo_rows(cells, width):
    parts = [row_from(cells, -d) for d in range(width, 0, -1)]
    parts += [cells] + [row_from(cells, d) for d in range(1, width + 1)]
    return jnp.concatenate(parts, axis=1)


def swap_halves(v):
    return lax.ppermute(v, "zh", [(0, 1), (1, 0)])


def pad_sides(values):
    return jnp.pad(values, ((1, 1), (0, 0), (1, 1), (0, 0)))


def tap_windows(padded, frame_count, row_count, col_count):
    windows = []
    for depth_off in range(3):
        for row_off in range(3):
            for col_off in range(3):
                window = padded[
                    depth_off : depth_off + frame_count,
                    row_off : row_off + row_count,
                    col_off : col_off + col_count,
                ]
                windows.append(window.reshape(frame_count * row_count * col_count, padded.shape[3]))
    return windows


def tap_sum(padded, kernel, frame_count, row_count, col_count):
    accum = None
    for tap_index, flat in enumerate(tap_windows(padded, frame_count, row_count, col_count)):
        term = jnp.dot(flat, kernel[tap_index], preferred_element_type=jnp.float32)
        accum = term if accum is None else accum + term
    return accum


def conv3(padded, kernel):
    taps = kernel.reshape(3, 3, 3, kernel.shape[1], kernel.shape[2])
    out = lax.conv_general_dilated(
        padded[None],
        taps,
        (1, 1, 1),
        "VALID",
        dimension_numbers=("NDHWC", "DHWIO", "NDHWC"),
        preferred_element_type=jnp.float32,
    )
    return out[0]


def gather_channels(latent):
    other = swap_halves(latent)
    half = lax.axis_index("zh")
    pair = jnp.where(half == 0, jnp.stack([latent, other]), jnp.stack([other, latent]))
    inner_count = lax.axis_size("inner")
    copies = jnp.broadcast_to(pair[None], (inner_count,) + pair.shape)
    inner = lax.all_to_all(copies, "inner", 0, 0, tiled=True)
    frame_count, row_count, col_count, own_chan = latent.shape
    total = inner.shape[0] * HALVES * own_chan
    return jnp.transpose(inner, (2, 3, 4, 1, 0, 5)).reshape(frame_count, row_count, col_count, total)


def reduce_channels(partial, own_chan):
    inner_count = lax.axis_size("inner")
    cells = partial.shape[1]
    blocks = partial.reshape(HALVES, inner_count, own_chan, cells).transpose(1, 0, 2, 3)
    sums = lax.all_to_all(blocks, "inner", 0, 0, tiled=True).sum(0)
    half = lax.axis_index("zh")
    mine = jnp.where(half == 0, sums[0], sums[1])
    theirs = jnp.where(half == 0, sums[1], sums[0])
    return mine + swap_halves(theirs)


def local(latent, conv_one, bias_one, conv_two, bias_two):
    frame_count, row_count, col_count, own_chan = latent.shape
    gathered = gather_channels(latent)
    extended = halo_rows(gathered, 2)
    first = conv3(pad_sides(extended), conv_one)
    hidden = jax.nn.relu(first + bias_one).astype(jnp.bfloat16)
    row = lax.axis_index("space") * row_count + jnp.arange(-1, row_count + 1)
    inside = (row >= 0) & (row < lax.axis_size("space") * row_count)
    hidden_ext = jnp.where(inside[None, :, None, None], hidden, jnp.zeros_like(hidden))
    partial = conv3(pad_sides(hidden_ext), conv_two)
    partial = partial.reshape(frame_count * row_count * col_count, -1).T
    mine = reduce_channels(partial, own_chan)
    second = mine.T.reshape(frame_count, row_count, col_count, own_chan)
    summed = latent.astype(jnp.float32) + second + bias_two
    return summed.astype(jnp.bfloat16)


def solution(mesh):
    space, chan = mesh.shape["space"], mesh.shape["chan"]
    split = Mesh(mesh.devices.reshape(space, HALVES, chan // HALVES), ("space",) + CHAN)
    in_specs = (
        P(None, "space", None, CHAN),
        P(None, None, CHAN),
        P(CHAN),
        P(None, CHAN, None),
        P(CHAN),
    )
    out_specs = P(None, "space", None, CHAN)
    return jax.shard_map(local, mesh=split, in_specs=in_specs, out_specs=out_specs, check_vma=False)
```

```python
import jax
import jax.numpy as jnp
from jax import lax
from jax.sharding import Mesh
from jax.sharding import PartitionSpec as P

CHAN = ("zh", "inner")
HALVES = 2
RUN = 16


def row_from(cells, shift):
    rows = lax.axis_size("space")
    pairs = []
    for target in range(rows):
        source = target + shift
        if 0 <= source < rows:
            cross = source // RUN != target // RUN
            for half in range(HALVES):
                other = (HALVES - 1 - half) if cross else half
                pairs.append((source * HALVES + other, target * HALVES + half))
    return lax.ppermute(cells, ("space", "zh"), pairs)


def halo_rows(cells, width):
    parts = [row_from(cells, -d) for d in range(width, 0, -1)]
    parts += [cells] + [row_from(cells, d) for d in range(1, width + 1)]
    return jnp.concatenate(parts, axis=1)


def swap_halves(v):
    return lax.ppermute(v, "zh", [(0, 1), (1, 0)])


def pad_sides(values):
    return jnp.pad(values, ((1, 1), (0, 0), (1, 1), (0, 0)))


def tap_windows(padded, frame_count, row_count, col_count):
    windows = []
    for depth_off in range(3):
        for row_off in range(3):
            for col_off in range(3):
                window = padded[
                    depth_off : depth_off + frame_count,
                    row_off : row_off + row_count,
                    col_off : col_off + col_count,
                ]
                windows.append(window.reshape(frame_count * row_count * col_count, padded.shape[3]))
    return windows


def tap_sum(padded, kernel, frame_count, row_count, col_count):
    accum = None
    for tap_index, flat in enumerate(tap_windows(padded, frame_count, row_count, col_count)):
        term = jnp.dot(flat, kernel[tap_index], preferred_element_type=jnp.float32)
        accum = term if accum is None else accum + term
    return accum


def conv3(padded, kernel):
    taps = kernel.reshape(3, 3, 3, kernel.shape[1], kernel.shape[2])
    out = lax.conv_general_dilated(
        padded[None],
        taps,
        (1, 1, 1),
        "VALID",
        dimension_numbers=("NDHWC", "DHWIO", "NDHWC"),
        preferred_element_type=jnp.float32,
    )
    return out[0]


def gather_channels(latent):
    other = swap_halves(latent)
    half = lax.axis_index("zh")
    pair = jnp.where(half == 0, jnp.stack([latent, other], 3), jnp.stack([other, latent], 3))
    inner_count = lax.axis_size("inner")
    copies = jnp.broadcast_to(pair[:, :, :, :, None], pair.shape[:4] + (inner_count,) + pair.shape[4:])
    inner = lax.all_to_all(copies, "inner", 4, 4, tiled=True)
    return inner.reshape(inner.shape[:3] + (-1,))


def reduce_channels(partial, own_chan):
    inner_count = lax.axis_size("inner")
    blocks = partial.reshape(partial.shape[0], HALVES, inner_count, own_chan)
    sums = lax.all_to_all(blocks, "inner", 2, 2, tiled=True).sum(2)
    half = lax.axis_index("zh")
    mine = jnp.where(half == 0, sums[:, 0], sums[:, 1])
    theirs = jnp.where(half == 0, sums[:, 1], sums[:, 0])
    return mine + swap_halves(theirs)


def local(latent, conv_one, bias_one, conv_two, bias_two):
    frame_count, row_count, col_count, own_chan = latent.shape
    gathered = gather_channels(latent)
    extended = halo_rows(gathered, 2)
    first = conv3(pad_sides(extended), conv_one)
    hidden = jax.nn.relu(first + bias_one).astype(jnp.bfloat16)
    row = lax.axis_index("space") * row_count + jnp.arange(-1, row_count + 1)
    inside = (row >= 0) & (row < lax.axis_size("space") * row_count)
    hidden_ext = jnp.where(inside[None, :, None, None], hidden, jnp.zeros_like(hidden))
    partial = conv3(pad_sides(hidden_ext), conv_two)
    partial = partial.reshape(frame_count * row_count * col_count, -1)
    mine = reduce_channels(partial, own_chan)
    second = mine.reshape(frame_count, row_count, col_count, own_chan)
    summed = latent.astype(jnp.float32) + second + bias_two
    return summed.astype(jnp.bfloat16)


def solution(mesh):
    space, chan = mesh.shape["space"], mesh.shape["chan"]
    split = Mesh(mesh.devices.reshape(space, HALVES, chan // HALVES), ("space",) + CHAN)
    in_specs = (
        P(None, "space", None, CHAN),
        P(None, None, CHAN),
        P(CHAN),
        P(None, CHAN, None),
        P(CHAN),
    )
    out_specs = P(None, "space", None, CHAN)
    return jax.shard_map(local, mesh=split, in_specs=in_specs, out_specs=out_specs, check_vma=False)
```

```python
import jax
import jax.numpy as jnp
from jax import lax
from jax.sharding import Mesh
from jax.sharding import PartitionSpec as P

CHAN = ("zh", "inner")
HALVES = 2
RUN = 16


def row_from(cells, shift):
    rows = lax.axis_size("space")
    pairs = []
    for target in range(rows):
        source = target + shift
        if 0 <= source < rows:
            cross = source // RUN != target // RUN
            for half in range(HALVES):
                other = (HALVES - 1 - half) if cross else half
                pairs.append((source * HALVES + other, target * HALVES + half))
    return lax.ppermute(cells, ("space", "zh"), pairs)


def halo_rows(cells, width):
    parts = [row_from(cells, -d) for d in range(width, 0, -1)]
    parts += [cells] + [row_from(cells, d) for d in range(1, width + 1)]
    return jnp.concatenate(parts, axis=1)


def swap_halves(v):
    return lax.ppermute(v, "zh", [(0, 1), (1, 0)])


def pad_sides(values):
    return jnp.pad(values, ((1, 1), (0, 0), (1, 1), (0, 0)))


def tap_windows(padded, frame_count, row_count, col_count):
    windows = []
    for depth_off in range(3):
        for row_off in range(3):
            for col_off in range(3):
                window = padded[
                    depth_off : depth_off + frame_count,
                    row_off : row_off + row_count,
                    col_off : col_off + col_count,
                ]
                windows.append(window.reshape(frame_count * row_count * col_count, padded.shape[3]))
    return windows


def tap_sum(padded, kernel, frame_count, row_count, col_count):
    accum = None
    for tap_index, flat in enumerate(tap_windows(padded, frame_count, row_count, col_count)):
        term = jnp.dot(flat, kernel[tap_index], preferred_element_type=jnp.float32)
        accum = term if accum is None else accum + term
    return accum


def conv3(padded, kernel):
    taps = kernel.reshape(3, 3, 3, kernel.shape[1], kernel.shape[2])
    out = lax.conv_general_dilated(
        padded[None],
        taps,
        (1, 1, 1),
        "VALID",
        dimension_numbers=("NDHWC", "DHWIO", "NDHWC"),
        preferred_element_type=jnp.float32,
    )
    return out[0]


def gather_channels(latent):
    other = swap_halves(latent)
    half = lax.axis_index("zh")
    pair = jnp.where(half == 0, jnp.stack([latent, other], 3), jnp.stack([other, latent], 3))
    inner_count = lax.axis_size("inner")
    copies = jnp.broadcast_to(pair[:, :, :, :, None], pair.shape[:4] + (inner_count,) + pair.shape[4:])
    inner = lax.all_to_all(copies, "inner", 4, 4, tiled=True)
    return inner.reshape(inner.shape[:3] + (-1,))


def reduce_channels(partial, own_chan):
    inner_count = lax.axis_size("inner")
    idx = lax.axis_index("inner")
    cur = partial.reshape(partial.shape[0], HALVES, -1)
    step = inner_count // 2
    while step >= 1:
        split = cur.reshape(cur.shape[0], HALVES, 2, -1)
        upper = (idx // step) % 2 == 1
        keep = jnp.where(upper, split[:, :, 1], split[:, :, 0])
        send = jnp.where(upper, split[:, :, 0], split[:, :, 1])
        cur = keep + lax.ppermute(send, "inner", [(i, i ^ step) for i in range(inner_count)])
        step //= 2
    half = lax.axis_index("zh")
    mine = jnp.where(half == 0, cur[:, 0], cur[:, 1])
    theirs = jnp.where(half == 0, cur[:, 1], cur[:, 0])
    return mine + swap_halves(theirs)


def local(latent, conv_one, bias_one, conv_two, bias_two):
    frame_count, row_count, col_count, own_chan = latent.shape
    gathered = gather_channels(latent)
    extended = halo_rows(gathered, 2)
    first = conv3(pad_sides(extended), conv_one)
    hidden = jax.nn.relu(first + bias_one).astype(jnp.bfloat16)
    row = lax.axis_index("space") * row_count + jnp.arange(-1, row_count + 1)
    inside = (row >= 0) & (row < lax.axis_size("space") * row_count)
    hidden_ext = jnp.where(inside[None, :, None, None], hidden, jnp.zeros_like(hidden))
    partial = conv3(pad_sides(hidden_ext), conv_two)
    partial = partial.reshape(frame_count * row_count * col_count, -1)
    mine = reduce_channels(partial, own_chan)
    second = mine.reshape(frame_count, row_count, col_count, own_chan)
    summed = latent.astype(jnp.float32) + second + bias_two
    return summed.astype(jnp.bfloat16)


def solution(mesh):
    space, chan = mesh.shape["space"], mesh.shape["chan"]
    split = Mesh(mesh.devices.reshape(space, HALVES, chan // HALVES), ("space",) + CHAN)
    in_specs = (
        P(None, "space", None, CHAN),
        P(None, None, CHAN),
        P(CHAN),
        P(None, CHAN, None),
        P(CHAN),
    )
    out_specs = P(None, "space", None, CHAN)
    return jax.shard_map(local, mesh=split, in_specs=in_specs, out_specs=out_specs, check_vma=False)
```

```python
import jax
import jax.numpy as jnp
from jax import lax
from jax.sharding import Mesh
from jax.sharding import PartitionSpec as P

CHAN = ("zh", "inner")
HALVES = 2
RUN = 16


def row_from(cells, shift):
    rows = lax.axis_size("space")
    pairs = []
    for target in range(rows):
        source = target + shift
        if 0 <= source < rows:
            cross = source // RUN != target // RUN
            for half in range(HALVES):
                other = (HALVES - 1 - half) if cross else half
                pairs.append((source * HALVES + other, target * HALVES + half))
    return lax.ppermute(cells, ("space", "zh"), pairs)


def halo_rows(cells, width):
    parts = [row_from(cells, -d) for d in range(width, 0, -1)]
    parts += [cells] + [row_from(cells, d) for d in range(1, width + 1)]
    return jnp.concatenate(parts, axis=1)


def swap_halves(v):
    return lax.ppermute(v, "zh", [(0, 1), (1, 0)])


def pad_sides(values):
    return jnp.pad(values, ((1, 1), (0, 0), (1, 1), (0, 0)))


def tap_windows(padded, frame_count, row_count, col_count):
    windows = []
    for depth_off in range(3):
        for row_off in range(3):
            for col_off in range(3):
                window = padded[
                    depth_off : depth_off + frame_count,
                    row_off : row_off + row_count,
                    col_off : col_off + col_count,
                ]
                windows.append(window.reshape(frame_count * row_count * col_count, padded.shape[3]))
    return windows


def tap_sum(padded, kernel, frame_count, row_count, col_count):
    accum = None
    for tap_index, flat in enumerate(tap_windows(padded, frame_count, row_count, col_count)):
        term = jnp.dot(flat, kernel[tap_index], preferred_element_type=jnp.float32)
        accum = term if accum is None else accum + term
    return accum


def conv3(padded, kernel):
    taps = kernel.reshape(3, 3, 3, kernel.shape[1], kernel.shape[2])
    out = lax.conv_general_dilated(
        padded[None],
        taps,
        (1, 1, 1),
        "VALID",
        dimension_numbers=("NDHWC", "DHWIO", "NDHWC"),
        preferred_element_type=jnp.float32,
    )
    return out[0]


def gather_channels(latent):
    other = swap_halves(latent)
    half = lax.axis_index("zh")
    pair = jnp.where(half == 0, jnp.stack([latent, other]), jnp.stack([other, latent]))
    inner = lax.all_gather(pair, "inner", axis=0, tiled=False)
    frame_count, row_count, col_count, own_chan = latent.shape
    total = inner.shape[0] * HALVES * own_chan
    return jnp.transpose(inner, (2, 3, 4, 1, 0, 5)).reshape(frame_count, row_count, col_count, total)


def reduce_channels(partial, own_chan):
    inner_count = lax.axis_size("inner")
    blocks = partial.reshape(partial.shape[0], HALVES, inner_count, own_chan)
    sums = lax.all_to_all(blocks, "inner", 2, 2, tiled=True).sum(2)
    half = lax.axis_index("zh")
    mine = jnp.where(half == 0, sums[:, 0], sums[:, 1])
    theirs = jnp.where(half == 0, sums[:, 1], sums[:, 0])
    return mine + swap_halves(theirs)


def local(latent, conv_one, bias_one, conv_two, bias_two):
    frame_count, row_count, col_count, own_chan = latent.shape
    gathered = gather_channels(latent)
    extended = halo_rows(gathered, 2)
    first = conv3(pad_sides(extended), conv_one)
    hidden = jax.nn.relu(first + bias_one).astype(jnp.bfloat16)
    row = lax.axis_index("space") * row_count + jnp.arange(-1, row_count + 1)
    inside = (row >= 0) & (row < lax.axis_size("space") * row_count)
    hidden_ext = jnp.where(inside[None, :, None, None], hidden, jnp.zeros_like(hidden))
    partial = conv3(pad_sides(hidden_ext), conv_two)
    partial = partial.reshape(frame_count * row_count * col_count, -1)
    mine = reduce_channels(partial, own_chan)
    second = mine.reshape(frame_count, row_count, col_count, own_chan)
    summed = latent.astype(jnp.float32) + second + bias_two
    return summed.astype(jnp.bfloat16)


def solution(mesh):
    space, chan = mesh.shape["space"], mesh.shape["chan"]
    split = Mesh(mesh.devices.reshape(space, HALVES, chan // HALVES), ("space",) + CHAN)
    in_specs = (
        P(None, "space", None, CHAN),
        P(None, None, CHAN),
        P(CHAN),
        P(None, CHAN, None),
        P(CHAN),
    )
    out_specs = P(None, "space", None, CHAN)
    return jax.shard_map(local, mesh=split, in_specs=in_specs, out_specs=out_specs, check_vma=False)
```

```python
import jax
import jax.numpy as jnp
from jax import lax
from jax.sharding import Mesh
from jax.sharding import PartitionSpec as P

CHAN = ("zh", "inner")
HALVES = 2
RUN = 16


def row_from(cells, shift):
    rows = lax.axis_size("space")
    pairs = []
    for target in range(rows):
        source = target + shift
        if 0 <= source < rows:
            cross = source // RUN != target // RUN
            for half in range(HALVES):
                other = (HALVES - 1 - half) if cross else half
                pairs.append((source * HALVES + other, target * HALVES + half))
    return lax.ppermute(cells, ("space", "zh"), pairs)


def halo_rows(cells, width):
    parts = [row_from(cells, -d) for d in range(width, 0, -1)]
    parts += [cells] + [row_from(cells, d) for d in range(1, width + 1)]
    return jnp.concatenate(parts, axis=1)


def swap_halves(v):
    return lax.ppermute(v, "zh", [(0, 1), (1, 0)])


def pad_sides(values):
    return jnp.pad(values, ((1, 1), (0, 0), (1, 1), (0, 0)))


def tap_windows(padded, frame_count, row_count, col_count):
    windows = []
    for depth_off in range(3):
        for row_off in range(3):
            for col_off in range(3):
                window = padded[
                    depth_off : depth_off + frame_count,
                    row_off : row_off + row_count,
                    col_off : col_off + col_count,
                ]
                windows.append(window.reshape(frame_count * row_count * col_count, padded.shape[3]))
    return windows


def tap_sum(padded, kernel, frame_count, row_count, col_count):
    accum = None
    for tap_index, flat in enumerate(tap_windows(padded, frame_count, row_count, col_count)):
        term = jnp.dot(flat, kernel[tap_index], preferred_element_type=jnp.float32)
        accum = term if accum is None else accum + term
    return accum


def conv3(padded, kernel):
    taps = kernel.reshape(3, 3, 3, kernel.shape[1], kernel.shape[2])
    out = lax.conv_general_dilated(
        padded[None],
        taps,
        (1, 1, 1),
        "VALID",
        dimension_numbers=("NDHWC", "DHWIO", "NDHWC"),
        preferred_element_type=jnp.float32,
    )
    return out[0]


def gather_channels(latent):
    other = swap_halves(latent)
    half = lax.axis_index("zh")
    pair = jnp.where(half == 0, jnp.stack([latent, other]), jnp.stack([other, latent]))
    inner = lax.all_gather(pair, "inner", axis=0, tiled=False)
    frame_count, row_count, col_count, own_chan = latent.shape
    total = inner.shape[0] * HALVES * own_chan
    return jnp.transpose(inner, (2, 3, 4, 1, 0, 5)).reshape(frame_count, row_count, col_count, total)


def reduce_channels(partial, own_chan):
    inner_count = lax.axis_size("inner")
    cells = partial.shape[0]
    blocks = partial.reshape(cells, HALVES, inner_count, own_chan).transpose(2, 0, 1, 3)
    blocks = blocks.reshape(inner_count, cells, HALVES * own_chan)
    sums = lax.all_to_all(blocks, "inner", 0, 0, tiled=True).sum(0)
    half = lax.axis_index("zh")
    low, high = sums[:, :own_chan], sums[:, own_chan:]
    mine = jnp.where(half == 0, low, high)
    theirs = jnp.where(half == 0, high, low)
    return mine + swap_halves(theirs)


def local(latent, conv_one, bias_one, conv_two, bias_two):
    frame_count, row_count, col_count, own_chan = latent.shape
    gathered = gather_channels(latent)
    extended = halo_rows(gathered, 2)
    first = conv3(pad_sides(extended), conv_one)
    hidden = jax.nn.relu(first + bias_one).astype(jnp.bfloat16)
    row = lax.axis_index("space") * row_count + jnp.arange(-1, row_count + 1)
    inside = (row >= 0) & (row < lax.axis_size("space") * row_count)
    hidden_ext = jnp.where(inside[None, :, None, None], hidden, jnp.zeros_like(hidden))
    partial = conv3(pad_sides(hidden_ext), conv_two)
    partial = partial.reshape(frame_count * row_count * col_count, -1)
    mine = reduce_channels(partial, own_chan)
    second = mine.reshape(frame_count, row_count, col_count, own_chan)
    summed = latent.astype(jnp.float32) + second + bias_two
    return summed.astype(jnp.bfloat16)


def solution(mesh):
    space, chan = mesh.shape["space"], mesh.shape["chan"]
    split = Mesh(mesh.devices.reshape(space, HALVES, chan // HALVES), ("space",) + CHAN)
    in_specs = (
        P(None, "space", None, CHAN),
        P(None, None, CHAN),
        P(CHAN),
        P(None, CHAN, None),
        P(CHAN),
    )
    out_specs = P(None, "space", None, CHAN)
    return jax.shard_map(local, mesh=split, in_specs=in_specs, out_specs=out_specs, check_vma=False)
```

```python
import jax
import jax.numpy as jnp
from jax import lax
from jax.sharding import Mesh
from jax.sharding import PartitionSpec as P

CHAN = ("zh", "inner")
HALVES = 2
RUN = 16


def row_from(cells, shift):
    rows = lax.axis_size("space")
    pairs = []
    for target in range(rows):
        source = target + shift
        if 0 <= source < rows:
            cross = source // RUN != target // RUN
            for half in range(HALVES):
                other = (HALVES - 1 - half) if cross else half
                pairs.append((source * HALVES + other, target * HALVES + half))
    return lax.ppermute(cells, ("space", "zh"), pairs)


def halo_rows(cells, width):
    parts = [row_from(cells, -d) for d in range(width, 0, -1)]
    parts += [cells] + [row_from(cells, d) for d in range(1, width + 1)]
    return jnp.concatenate(parts, axis=1)


def swap_halves(v):
    return lax.ppermute(v, "zh", [(0, 1), (1, 0)])


def pad_sides(values):
    return jnp.pad(values, ((1, 1), (0, 0), (1, 1), (0, 0)))


def tap_windows(padded, frame_count, row_count, col_count):
    windows = []
    for depth_off in range(3):
        for row_off in range(3):
            for col_off in range(3):
                window = padded[
                    depth_off : depth_off + frame_count,
                    row_off : row_off + row_count,
                    col_off : col_off + col_count,
                ]
                windows.append(window.reshape(frame_count * row_count * col_count, padded.shape[3]))
    return windows


def tap_sum(padded, kernel, frame_count, row_count, col_count):
    accum = None
    for tap_index, flat in enumerate(tap_windows(padded, frame_count, row_count, col_count)):
        term = jnp.dot(flat, kernel[tap_index], preferred_element_type=jnp.float32)
        accum = term if accum is None else accum + term
    return accum


def conv3(padded, kernel):
    taps = kernel.reshape(3, 3, 3, kernel.shape[1], kernel.shape[2])
    out = lax.conv_general_dilated(
        padded[None],
        taps,
        (1, 1, 1),
        "VALID",
        dimension_numbers=("NDHWC", "DHWIO", "NDHWC"),
        preferred_element_type=jnp.float32,
    )
    return out[0]


def gather_channels(latent):
    other = swap_halves(latent)
    half = lax.axis_index("zh")
    pair = jnp.where(half == 0, jnp.stack([latent, other]), jnp.stack([other, latent]))
    inner = lax.all_gather(pair, "inner", axis=0, tiled=False)
    frame_count, row_count, col_count, own_chan = latent.shape
    total = inner.shape[0] * HALVES * own_chan
    return jnp.transpose(inner, (2, 3, 4, 1, 0, 5)).reshape(frame_count, row_count, col_count, total)


def reduce_channels(partial, own_chan):
    inner_count = lax.axis_size("inner")
    cells = partial.shape[0]
    blocks = partial.reshape(cells, HALVES, inner_count, own_chan).transpose(2, 0, 1, 3)
    blocks = blocks.reshape(inner_count, cells, HALVES * own_chan)
    sums = lax.all_to_all(blocks, "inner", 0, 0, tiled=True).sum(0)
    half = lax.axis_index("zh")
    low, high = sums[:, :own_chan], sums[:, own_chan:]
    mine = jnp.where(half == 0, low, high)
    theirs = jnp.where(half == 0, high, low)
    return mine + swap_halves(theirs.astype(jnp.bfloat16)).astype(jnp.float32)


def local(latent, conv_one, bias_one, conv_two, bias_two):
    frame_count, row_count, col_count, own_chan = latent.shape
    gathered = gather_channels(latent)
    extended = halo_rows(gathered, 2)
    first = conv3(pad_sides(extended), conv_one)
    hidden = jax.nn.relu(first + bias_one).astype(jnp.bfloat16)
    row = lax.axis_index("space") * row_count + jnp.arange(-1, row_count + 1)
    inside = (row >= 0) & (row < lax.axis_size("space") * row_count)
    hidden_ext = jnp.where(inside[None, :, None, None], hidden, jnp.zeros_like(hidden))
    partial = conv3(pad_sides(hidden_ext), conv_two)
    partial = partial.reshape(frame_count * row_count * col_count, -1)
    mine = reduce_channels(partial, own_chan)
    second = mine.reshape(frame_count, row_count, col_count, own_chan)
    summed = latent.astype(jnp.float32) + second + bias_two
    return summed.astype(jnp.bfloat16)


def solution(mesh):
    space, chan = mesh.shape["space"], mesh.shape["chan"]
    split = Mesh(mesh.devices.reshape(space, HALVES, chan // HALVES), ("space",) + CHAN)
    in_specs = (
        P(None, "space", None, CHAN),
        P(None, None, CHAN),
        P(CHAN),
        P(None, CHAN, None),
        P(CHAN),
    )
    out_specs = P(None, "space", None, CHAN)
    return jax.shard_map(local, mesh=split, in_specs=in_specs, out_specs=out_specs, check_vma=False)
```

```python
import jax
import jax.numpy as jnp
from jax import lax
from jax.sharding import Mesh
from jax.sharding import PartitionSpec as P

CHAN = ("zh", "inner")
HALVES = 2
RUN = 16


def row_from(cells, shift):
    rows = lax.axis_size("space")
    pairs = []
    for target in range(rows):
        source = target + shift
        if 0 <= source < rows:
            cross = source // RUN != target // RUN
            for half in range(HALVES):
                other = (HALVES - 1 - half) if cross else half
                pairs.append((source * HALVES + other, target * HALVES + half))
    return lax.ppermute(cells, ("space", "zh"), pairs)


def halo_rows(cells, width):
    parts = [row_from(cells, -d) for d in range(width, 0, -1)]
    parts += [cells] + [row_from(cells, d) for d in range(1, width + 1)]
    return jnp.concatenate(parts, axis=1)


def swap_halves(v):
    return lax.ppermute(v, "zh", [(0, 1), (1, 0)])


def pad_sides(values):
    return jnp.pad(values, ((1, 1), (0, 0), (1, 1), (0, 0)))


def tap_windows(padded, frame_count, row_count, col_count):
    windows = []
    for depth_off in range(3):
        for row_off in range(3):
            for col_off in range(3):
                window = padded[
                    depth_off : depth_off + frame_count,
                    row_off : row_off + row_count,
                    col_off : col_off + col_count,
                ]
                windows.append(window.reshape(frame_count * row_count * col_count, padded.shape[3]))
    return windows


def tap_sum(padded, kernel, frame_count, row_count, col_count):
    accum = None
    for tap_index, flat in enumerate(tap_windows(padded, frame_count, row_count, col_count)):
        term = jnp.dot(flat, kernel[tap_index], preferred_element_type=jnp.float32)
        accum = term if accum is None else accum + term
    return accum


def conv3(padded, kernel):
    taps = kernel.reshape(3, 3, 3, kernel.shape[1], kernel.shape[2])
    out = lax.conv_general_dilated(
        padded[None],
        taps,
        (1, 1, 1),
        ((1, 1), (0, 0), (1, 1)),
        dimension_numbers=("NDHWC", "DHWIO", "NDHWC"),
        preferred_element_type=jnp.float32,
    )
    return out[0]


def gather_channels(latent):
    other = swap_halves(latent)
    half = lax.axis_index("zh")
    pair = jnp.where(half == 0, jnp.stack([latent, other]), jnp.stack([other, latent]))
    inner = lax.all_gather(pair, "inner", axis=0, tiled=False)
    frame_count, row_count, col_count, own_chan = latent.shape
    total = inner.shape[0] * HALVES * own_chan
    return jnp.transpose(inner, (2, 3, 4, 1, 0, 5)).reshape(frame_count, row_count, col_count, total)


def reduce_channels(partial, own_chan):
    inner_count = lax.axis_size("inner")
    cells = partial.shape[0]
    blocks = partial.reshape(cells, HALVES, inner_count, own_chan).transpose(2, 0, 1, 3)
    blocks = blocks.reshape(inner_count, cells, HALVES * own_chan)
    sums = lax.all_to_all(blocks, "inner", 0, 0, tiled=True).sum(0)
    half = lax.axis_index("zh")
    low, high = sums[:, :own_chan], sums[:, own_chan:]
    mine = jnp.where(half == 0, low, high)
    theirs = jnp.where(half == 0, high, low)
    return mine + swap_halves(theirs)


def local(latent, conv_one, bias_one, conv_two, bias_two):
    frame_count, row_count, col_count, own_chan = latent.shape
    gathered = gather_channels(latent)
    extended = halo_rows(gathered, 2)
    first = conv3(extended, conv_one)
    hidden = jax.nn.relu(first + bias_one).astype(jnp.bfloat16)
    row = lax.axis_index("space") * row_count + jnp.arange(-1, row_count + 1)
    inside = (row >= 0) & (row < lax.axis_size("space") * row_count)
    hidden_ext = jnp.where(inside[None, :, None, None], hidden, jnp.zeros_like(hidden))
    partial = conv3(hidden_ext, conv_two)
    partial = partial.reshape(frame_count * row_count * col_count, -1)
    mine = reduce_channels(partial, own_chan)
    second = mine.reshape(frame_count, row_count, col_count, own_chan)
    summed = latent.astype(jnp.float32) + second + bias_two
    return summed.astype(jnp.bfloat16)


def solution(mesh):
    space, chan = mesh.shape["space"], mesh.shape["chan"]
    split = Mesh(mesh.devices.reshape(space, HALVES, chan // HALVES), ("space",) + CHAN)
    in_specs = (
        P(None, "space", None, CHAN),
        P(None, None, CHAN),
        P(CHAN),
        P(None, CHAN, None),
        P(CHAN),
    )
    out_specs = P(None, "space", None, CHAN)
    return jax.shard_map(local, mesh=split, in_specs=in_specs, out_specs=out_specs, check_vma=False)
```

```python
import jax
import jax.numpy as jnp
from jax import lax
from jax.sharding import Mesh
from jax.sharding import PartitionSpec as P

CHAN = ("zh", "inner")
HALVES = 2
RUN = 16


def row_from(cells, shift):
    rows = lax.axis_size("space")
    pairs = []
    for target in range(rows):
        source = target + shift
        if 0 <= source < rows:
            cross = source // RUN != target // RUN
            for half in range(HALVES):
                other = (HALVES - 1 - half) if cross else half
                pairs.append((source * HALVES + other, target * HALVES + half))
    return lax.ppermute(cells, ("space", "zh"), pairs)


def halo_rows(cells, width, axis):
    parts = [row_from(cells, -d) for d in range(width, 0, -1)]
    parts += [cells] + [row_from(cells, d) for d in range(1, width + 1)]
    return jnp.concatenate(parts, axis=axis)


def swap_halves(v):
    return lax.ppermute(v, "zh", [(0, 1), (1, 0)])


def pad_sides(values):
    return jnp.pad(values, ((1, 1), (0, 0), (1, 1), (0, 0)))


def tap_windows(padded, frame_count, row_count, col_count):
    windows = []
    for depth_off in range(3):
        for row_off in range(3):
            for col_off in range(3):
                window = padded[
                    depth_off : depth_off + frame_count,
                    row_off : row_off + row_count,
                    col_off : col_off + col_count,
                ]
                windows.append(window.reshape(frame_count * row_count * col_count, padded.shape[3]))
    return windows


def tap_sum(padded, kernel, frame_count, row_count, col_count):
    accum = None
    for tap_index, flat in enumerate(tap_windows(padded, frame_count, row_count, col_count)):
        term = jnp.dot(flat, kernel[tap_index], preferred_element_type=jnp.float32)
        accum = term if accum is None else accum + term
    return accum


def conv3(padded, kernel):
    taps = kernel.reshape(3, 3, 3, kernel.shape[1], kernel.shape[2])
    out = lax.conv_general_dilated(
        padded[None],
        taps,
        (1, 1, 1),
        ((1, 1), (0, 0), (1, 1)),
        dimension_numbers=("NDHWC", "DHWIO", "NDHWC"),
        preferred_element_type=jnp.float32,
    )
    return out[0]


def gather_channels(latent, width):
    other = swap_halves(latent)
    half = lax.axis_index("zh")
    pair = jnp.where(half == 0, jnp.stack([latent, other]), jnp.stack([other, latent]))
    pair = halo_rows(pair, width, 2)
    inner = lax.all_gather(pair, "inner", axis=0, tiled=False)
    frame_count, row_count, col_count, own_chan = inner.shape[2:]
    total = inner.shape[0] * HALVES * own_chan
    return jnp.transpose(inner, (2, 3, 4, 1, 0, 5)).reshape(frame_count, row_count, col_count, total)


def reduce_channels(partial, own_chan):
    inner_count = lax.axis_size("inner")
    cells = partial.shape[0]
    blocks = partial.reshape(cells, HALVES, inner_count, own_chan).transpose(2, 0, 1, 3)
    blocks = blocks.reshape(inner_count, cells, HALVES * own_chan)
    sums = lax.all_to_all(blocks, "inner", 0, 0, tiled=True).sum(0)
    half = lax.axis_index("zh")
    low, high = sums[:, :own_chan], sums[:, own_chan:]
    mine = jnp.where(half == 0, low, high)
    theirs = jnp.where(half == 0, high, low)
    return mine + swap_halves(theirs)


def local(latent, conv_one, bias_one, conv_two, bias_two):
    frame_count, row_count, col_count, own_chan = latent.shape
    extended = gather_channels(latent, 2)
    first = conv3(extended, conv_one)
    hidden = jax.nn.relu(first + bias_one).astype(jnp.bfloat16)
    row = lax.axis_index("space") * row_count + jnp.arange(-1, row_count + 1)
    inside = (row >= 0) & (row < lax.axis_size("space") * row_count)
    hidden_ext = jnp.where(inside[None, :, None, None], hidden, jnp.zeros_like(hidden))
    partial = conv3(hidden_ext, conv_two)
    partial = partial.reshape(frame_count * row_count * col_count, -1)
    mine = reduce_channels(partial, own_chan)
    second = mine.reshape(frame_count, row_count, col_count, own_chan)
    summed = latent.astype(jnp.float32) + second + bias_two
    return summed.astype(jnp.bfloat16)


def solution(mesh):
    space, chan = mesh.shape["space"], mesh.shape["chan"]
    split = Mesh(mesh.devices.reshape(space, HALVES, chan // HALVES), ("space",) + CHAN)
    in_specs = (
        P(None, "space", None, CHAN),
        P(None, None, CHAN),
        P(CHAN),
        P(None, CHAN, None),
        P(CHAN),
    )
    out_specs = P(None, "space", None, CHAN)
    return jax.shard_map(local, mesh=split, in_specs=in_specs, out_specs=out_specs, check_vma=False)
```

```python
import jax
import jax.numpy as jnp
from jax import lax
from jax.sharding import Mesh
from jax.sharding import PartitionSpec as P

CHAN = ("zh", "inner")
HALVES = 2
RUN = 16


def row_from(cells, shift):
    rows = lax.axis_size("space")
    pairs = []
    for target in range(rows):
        source = target + shift
        if 0 <= source < rows:
            cross = source // RUN != target // RUN
            for half in range(HALVES):
                other = (HALVES - 1 - half) if cross else half
                pairs.append((source * HALVES + other, target * HALVES + half))
    return lax.ppermute(cells, ("space", "zh"), pairs)


def halo_rows(cells, width):
    parts = [row_from(cells, -d) for d in range(width, 0, -1)]
    parts += [cells] + [row_from(cells, d) for d in range(1, width + 1)]
    return jnp.concatenate(parts, axis=1)


def swap_halves(v):
    return lax.ppermute(v, "zh", [(0, 1), (1, 0)])


def pad_sides(values):
    return jnp.pad(values, ((1, 1), (0, 0), (1, 1), (0, 0)))


def tap_windows(padded, frame_count, row_count, col_count):
    windows = []
    for depth_off in range(3):
        for row_off in range(3):
            for col_off in range(3):
                window = padded[
                    depth_off : depth_off + frame_count,
                    row_off : row_off + row_count,
                    col_off : col_off + col_count,
                ]
                windows.append(window.reshape(frame_count * row_count * col_count, padded.shape[3]))
    return windows


def tap_sum(padded, kernel, frame_count, row_count, col_count):
    accum = None
    for tap_index, flat in enumerate(tap_windows(padded, frame_count, row_count, col_count)):
        term = jnp.dot(flat, kernel[tap_index], preferred_element_type=jnp.float32)
        accum = term if accum is None else accum + term
    return accum


def conv3(padded, kernel):
    taps = kernel.reshape(3, 3, 3, kernel.shape[1], kernel.shape[2])
    out = lax.conv_general_dilated(
        padded[None],
        taps,
        (1, 1, 1),
        ((1, 1), (0, 0), (1, 1)),
        dimension_numbers=("NDHWC", "DHWIO", "NDHWC"),
        preferred_element_type=jnp.float32,
    )
    return out[0]


def gather_channels(latent):
    pair = lax.all_gather(latent, "zh", axis=0, tiled=False)
    inner = lax.all_gather(pair, "inner", axis=0, tiled=False)
    frame_count, row_count, col_count, own_chan = latent.shape
    total = inner.shape[0] * HALVES * own_chan
    return jnp.transpose(inner, (2, 3, 4, 1, 0, 5)).reshape(frame_count, row_count, col_count, total)


def reduce_channels(partial, own_chan):
    inner_count = lax.axis_size("inner")
    cells = partial.shape[0]
    blocks = partial.reshape(cells, HALVES, inner_count, own_chan).transpose(2, 0, 1, 3)
    blocks = blocks.reshape(inner_count, cells, HALVES * own_chan)
    sums = lax.all_to_all(blocks, "inner", 0, 0, tiled=True).sum(0)
    half = lax.axis_index("zh")
    low, high = sums[:, :own_chan], sums[:, own_chan:]
    mine = jnp.where(half == 0, low, high)
    theirs = jnp.where(half == 0, high, low)
    return mine + swap_halves(theirs)


def local(latent, conv_one, bias_one, conv_two, bias_two):
    frame_count, row_count, col_count, own_chan = latent.shape
    gathered = gather_channels(latent)
    extended = halo_rows(gathered, 2)
    first = conv3(extended, conv_one)
    hidden = jax.nn.relu(first + bias_one).astype(jnp.bfloat16)
    row = lax.axis_index("space") * row_count + jnp.arange(-1, row_count + 1)
    inside = (row >= 0) & (row < lax.axis_size("space") * row_count)
    hidden_ext = jnp.where(inside[None, :, None, None], hidden, jnp.zeros_like(hidden))
    partial = conv3(hidden_ext, conv_two)
    partial = partial.reshape(frame_count * row_count * col_count, -1)
    mine = reduce_channels(partial, own_chan)
    second = mine.reshape(frame_count, row_count, col_count, own_chan)
    summed = latent.astype(jnp.float32) + second + bias_two
    return summed.astype(jnp.bfloat16)


def solution(mesh):
    space, chan = mesh.shape["space"], mesh.shape["chan"]
    split = Mesh(mesh.devices.reshape(space, HALVES, chan // HALVES), ("space",) + CHAN)
    in_specs = (
        P(None, "space", None, CHAN),
        P(None, None, CHAN),
        P(CHAN),
        P(None, CHAN, None),
        P(CHAN),
    )
    out_specs = P(None, "space", None, CHAN)
    return jax.shard_map(local, mesh=split, in_specs=in_specs, out_specs=out_specs, check_vma=False)
```

```python
import jax
import jax.numpy as jnp
from jax import lax
from jax.sharding import Mesh
from jax.sharding import PartitionSpec as P

CHAN = ("zh", "inner")
HALVES = 2
RUN = 16


def row_from(cells, shift):
    rows = lax.axis_size("space")
    pairs = []
    for target in range(rows):
        source = target + shift
        if 0 <= source < rows:
            cross = source // RUN != target // RUN
            for half in range(HALVES):
                other = (HALVES - 1 - half) if cross else half
                pairs.append((source * HALVES + other, target * HALVES + half))
    return lax.ppermute(cells, ("space", "zh"), pairs)


def halo_rows(cells, width):
    parts = [row_from(cells, -d) for d in range(width, 0, -1)]
    parts += [cells] + [row_from(cells, d) for d in range(1, width + 1)]
    return jnp.concatenate(parts, axis=1)


def swap_halves(v):
    return lax.ppermute(v, "zh", [(0, 1), (1, 0)])


def pad_sides(values):
    return jnp.pad(values, ((1, 1), (0, 0), (1, 1), (0, 0)))


def tap_windows(padded, frame_count, row_count, col_count):
    windows = []
    for depth_off in range(3):
        for row_off in range(3):
            for col_off in range(3):
                window = padded[
                    depth_off : depth_off + frame_count,
                    row_off : row_off + row_count,
                    col_off : col_off + col_count,
                ]
                windows.append(window.reshape(frame_count * row_count * col_count, padded.shape[3]))
    return windows


def tap_sum(padded, kernel, frame_count, row_count, col_count):
    accum = None
    for tap_index, flat in enumerate(tap_windows(padded, frame_count, row_count, col_count)):
        term = jnp.dot(flat, kernel[tap_index], preferred_element_type=jnp.float32)
        accum = term if accum is None else accum + term
    return accum


def conv3(padded, kernel):
    taps = kernel.reshape(3, 3, 3, kernel.shape[1], kernel.shape[2])
    out = lax.conv_general_dilated(
        padded[None],
        taps,
        (1, 1, 1),
        ((1, 1), (0, 0), (1, 1)),
        dimension_numbers=("NDHWC", "DHWIO", "NDHWC"),
        preferred_element_type=jnp.float32,
    )
    return out[0]


def gather_channels(latent):
    pair = lax.all_gather(latent, "zh", axis=0, tiled=False)
    inner = lax.all_gather(pair, "inner", axis=0, tiled=False)
    frame_count, row_count, col_count, own_chan = latent.shape
    total = inner.shape[0] * HALVES * own_chan
    return jnp.transpose(inner, (2, 3, 4, 1, 0, 5)).reshape(frame_count, row_count, col_count, total)


def reduce_channels(partial, own_chan):
    inner_count = lax.axis_size("inner")
    cells = partial.shape[0]
    blocks = partial.reshape(cells, HALVES, inner_count, own_chan).transpose(2, 0, 1, 3)
    blocks = blocks.reshape(inner_count, cells, HALVES * own_chan)
    sums = lax.all_to_all(blocks, "inner", 0, 0, tiled=True).sum(0)
    half = lax.axis_index("zh")
    low, high = sums[:, :own_chan], sums[:, own_chan:]
    mine = jnp.where(half == 0, low, high)
    theirs = jnp.where(half == 0, high, low)
    both = lax.all_gather(theirs, "zh", axis=0, tiled=False)
    return mine + jnp.where(half == 0, both[1], both[0])


def local(latent, conv_one, bias_one, conv_two, bias_two):
    frame_count, row_count, col_count, own_chan = latent.shape
    gathered = gather_channels(latent)
    extended = halo_rows(gathered, 2)
    first = conv3(extended, conv_one)
    hidden = jax.nn.relu(first + bias_one).astype(jnp.bfloat16)
    row = lax.axis_index("space") * row_count + jnp.arange(-1, row_count + 1)
    inside = (row >= 0) & (row < lax.axis_size("space") * row_count)
    hidden_ext = jnp.where(inside[None, :, None, None], hidden, jnp.zeros_like(hidden))
    partial = conv3(hidden_ext, conv_two)
    partial = partial.reshape(frame_count * row_count * col_count, -1)
    mine = reduce_channels(partial, own_chan)
    second = mine.reshape(frame_count, row_count, col_count, own_chan)
    summed = latent.astype(jnp.float32) + second + bias_two
    return summed.astype(jnp.bfloat16)


def solution(mesh):
    space, chan = mesh.shape["space"], mesh.shape["chan"]
    split = Mesh(mesh.devices.reshape(space, HALVES, chan // HALVES), ("space",) + CHAN)
    in_specs = (
        P(None, "space", None, CHAN),
        P(None, None, CHAN),
        P(CHAN),
        P(None, CHAN, None),
        P(CHAN),
    )
    out_specs = P(None, "space", None, CHAN)
    return jax.shard_map(local, mesh=split, in_specs=in_specs, out_specs=out_specs, check_vma=False)
```

```python
import jax
import jax.numpy as jnp
from jax import lax
from jax.sharding import Mesh
from jax.sharding import PartitionSpec as P

CHAN = ("zh", "x", "core")
INNER = ("x", "core")
HALVES = 2
CORES = 2
RUN = 16


def row_from(cells, shift):
    rows = lax.axis_size("space")
    pairs = []
    for target in range(rows):
        source = target + shift
        if 0 <= source < rows:
            cross = source // RUN != target // RUN
            for half in range(HALVES):
                other = (HALVES - 1 - half) if cross else half
                pairs.append((source * HALVES + other, target * HALVES + half))
    return lax.ppermute(cells, ("space", "zh"), pairs)


def halo_rows(cells, width):
    parts = [row_from(cells, -d) for d in range(width, 0, -1)]
    parts += [cells] + [row_from(cells, d) for d in range(1, width + 1)]
    return jnp.concatenate(parts, axis=1)


def swap_halves(v):
    return lax.ppermute(v, "zh", [(0, 1), (1, 0)])


def pad_sides(values):
    return jnp.pad(values, ((1, 1), (0, 0), (1, 1), (0, 0)))


def tap_windows(padded, frame_count, row_count, col_count):
    windows = []
    for depth_off in range(3):
        for row_off in range(3):
            for col_off in range(3):
                window = padded[
                    depth_off : depth_off + frame_count,
                    row_off : row_off + row_count,
                    col_off : col_off + col_count,
                ]
                windows.append(window.reshape(frame_count * row_count * col_count, padded.shape[3]))
    return windows


def tap_sum(padded, kernel, frame_count, row_count, col_count):
    accum = None
    for tap_index, flat in enumerate(tap_windows(padded, frame_count, row_count, col_count)):
        term = jnp.dot(flat, kernel[tap_index], preferred_element_type=jnp.float32)
        accum = term if accum is None else accum + term
    return accum


def conv3(padded, kernel):
    taps = kernel.reshape(3, 3, 3, kernel.shape[1], kernel.shape[2])
    out = lax.conv_general_dilated(
        padded[None],
        taps,
        (1, 1, 1),
        ((1, 1), (0, 0), (1, 1)),
        dimension_numbers=("NDHWC", "DHWIO", "NDHWC"),
        preferred_element_type=jnp.float32,
    )
    return out[0]


def gather_channels(latent):
    pair = lax.all_gather(latent, "zh", axis=0, tiled=False)
    chip = lax.all_gather(pair, "core", axis=0, tiled=False)
    inner = lax.all_gather(chip, "x", axis=0, tiled=False)
    inner = inner.reshape((-1,) + inner.shape[2:])
    frame_count, row_count, col_count, own_chan = latent.shape
    total = inner.shape[0] * HALVES * own_chan
    return jnp.transpose(inner, (2, 3, 4, 1, 0, 5)).reshape(frame_count, row_count, col_count, total)


def reduce_channels(partial, own_chan):
    inner_count = lax.axis_size(INNER)
    cells = partial.shape[0]
    blocks = partial.reshape(cells, HALVES, inner_count, own_chan).transpose(2, 0, 1, 3)
    blocks = blocks.reshape(inner_count, cells, HALVES * own_chan)
    sums = lax.all_to_all(blocks, INNER, 0, 0, tiled=True).sum(0)
    half = lax.axis_index("zh")
    low, high = sums[:, :own_chan], sums[:, own_chan:]
    mine = jnp.where(half == 0, low, high)
    theirs = jnp.where(half == 0, high, low)
    both = lax.all_gather(theirs, "zh", axis=0, tiled=False)
    return mine + jnp.where(half == 0, both[1], both[0])


def local(latent, conv_one, bias_one, conv_two, bias_two):
    frame_count, row_count, col_count, own_chan = latent.shape
    gathered = gather_channels(latent)
    extended = halo_rows(gathered, 2)
    first = conv3(extended, conv_one)
    hidden = jax.nn.relu(first + bias_one).astype(jnp.bfloat16)
    row = lax.axis_index("space") * row_count + jnp.arange(-1, row_count + 1)
    inside = (row >= 0) & (row < lax.axis_size("space") * row_count)
    hidden_ext = jnp.where(inside[None, :, None, None], hidden, jnp.zeros_like(hidden))
    partial = conv3(hidden_ext, conv_two)
    partial = partial.reshape(frame_count * row_count * col_count, -1)
    mine = reduce_channels(partial, own_chan)
    second = mine.reshape(frame_count, row_count, col_count, own_chan)
    summed = latent.astype(jnp.float32) + second + bias_two
    return summed.astype(jnp.bfloat16)


def solution(mesh):
    space, chan = mesh.shape["space"], mesh.shape["chan"]
    split = Mesh(
        mesh.devices.reshape(space, HALVES, chan // (HALVES * CORES), CORES), ("space",) + CHAN
    )
    in_specs = (
        P(None, "space", None, CHAN),
        P(None, None, CHAN),
        P(CHAN),
        P(None, CHAN, None),
        P(CHAN),
    )
    out_specs = P(None, "space", None, CHAN)
    return jax.shard_map(local, mesh=split, in_specs=in_specs, out_specs=out_specs, check_vma=False)
```

```python
import jax
import jax.numpy as jnp
from jax import lax
from jax.sharding import Mesh
from jax.sharding import PartitionSpec as P

CHAN = ("zh", "inner")
HALVES = 2
RUN = 16


def row_from(cells, shift):
    rows = lax.axis_size("space")
    pairs = []
    for target in range(rows):
        source = target + shift
        if 0 <= source < rows:
            cross = source // RUN != target // RUN
            for half in range(HALVES):
                other = (HALVES - 1 - half) if cross else half
                pairs.append((source * HALVES + other, target * HALVES + half))
    return lax.ppermute(cells, ("space", "zh"), pairs)


def halo_rows(cells, width):
    parts = [row_from(cells, -d) for d in range(width, 0, -1)]
    parts += [cells] + [row_from(cells, d) for d in range(1, width + 1)]
    return jnp.concatenate(parts, axis=1)


def swap_halves(v):
    return lax.ppermute(v, "zh", [(0, 1), (1, 0)])


def pad_sides(values):
    return jnp.pad(values, ((1, 1), (0, 0), (1, 1), (0, 0)))


def tap_windows(padded, frame_count, row_count, col_count):
    windows = []
    for depth_off in range(3):
        for row_off in range(3):
            for col_off in range(3):
                window = padded[
                    depth_off : depth_off + frame_count,
                    row_off : row_off + row_count,
                    col_off : col_off + col_count,
                ]
                windows.append(window.reshape(frame_count * row_count * col_count, padded.shape[3]))
    return windows


def tap_sum(padded, kernel, frame_count, row_count, col_count):
    accum = None
    for tap_index, flat in enumerate(tap_windows(padded, frame_count, row_count, col_count)):
        term = jnp.dot(flat, kernel[tap_index], preferred_element_type=jnp.float32)
        accum = term if accum is None else accum + term
    return accum


def conv3(padded, kernel):
    taps = kernel.reshape(3, 3, 3, kernel.shape[1], kernel.shape[2])
    out = lax.conv_general_dilated(
        padded[None],
        taps,
        (1, 1, 1),
        ((1, 1), (0, 0), (1, 1)),
        dimension_numbers=("NDHWC", "DHWIO", "NDHWC"),
        preferred_element_type=jnp.float32,
    )
    return out[0]


def gather_channels(latent):
    pair = lax.all_gather(latent, "zh", axis=0, tiled=False)
    inner = lax.all_gather(pair, "inner", axis=0, tiled=False)
    frame_count, row_count, col_count, own_chan = latent.shape
    total = inner.shape[0] * HALVES * own_chan
    return jnp.transpose(inner, (2, 3, 4, 1, 0, 5)).reshape(frame_count, row_count, col_count, total)


def reduce_channels(partial, own_chan):
    inner_count = lax.axis_size("inner")
    cells = partial.shape[0]
    blocks = partial.reshape(cells, HALVES, inner_count, own_chan).transpose(2, 0, 1, 3)
    blocks = blocks.reshape(inner_count, cells, HALVES * own_chan)
    sums = lax.all_to_all(blocks, "inner", 0, 0, tiled=True).sum(0)
    half = lax.axis_index("zh")
    low, high = sums[:, :own_chan], sums[:, own_chan:]
    mine = jnp.where(half == 0, low, high)
    theirs = jnp.where(half == 0, high, low)
    dense = theirs.reshape(-1, 2 * theirs.shape[1])
    both = lax.all_gather(dense, "zh", axis=0, tiled=False).reshape((HALVES,) + theirs.shape)
    return mine + jnp.where(half == 0, both[1], both[0])


def local(latent, conv_one, bias_one, conv_two, bias_two):
    frame_count, row_count, col_count, own_chan = latent.shape
    gathered = gather_channels(latent)
    extended = halo_rows(gathered, 2)
    first = conv3(extended, conv_one)
    hidden = jax.nn.relu(first + bias_one).astype(jnp.bfloat16)
    row = lax.axis_index("space") * row_count + jnp.arange(-1, row_count + 1)
    inside = (row >= 0) & (row < lax.axis_size("space") * row_count)
    hidden_ext = jnp.where(inside[None, :, None, None], hidden, jnp.zeros_like(hidden))
    partial = conv3(hidden_ext, conv_two)
    partial = partial.reshape(frame_count * row_count * col_count, -1)
    mine = reduce_channels(partial, own_chan)
    second = mine.reshape(frame_count, row_count, col_count, own_chan)
    summed = latent.astype(jnp.float32) + second + bias_two
    return summed.astype(jnp.bfloat16)


def solution(mesh):
    space, chan = mesh.shape["space"], mesh.shape["chan"]
    split = Mesh(mesh.devices.reshape(space, HALVES, chan // HALVES), ("space",) + CHAN)
    in_specs = (
        P(None, "space", None, CHAN),
        P(None, None, CHAN),
        P(CHAN),
        P(None, CHAN, None),
        P(CHAN),
    )
    out_specs = P(None, "space", None, CHAN)
    return jax.shard_map(local, mesh=split, in_specs=in_specs, out_specs=out_specs, check_vma=False)
```
